256 devices in a mesh: run: 32 (over z, x_lo, core), entry: 8 (over x_hi, y).
Axes of the slice: x: 4 (x_hi: 2, x_lo: 2; x = x_hi * 2 + x_lo), y: 4, z: 8, core: 2. Of those that a mesh axis runs over, the one named last changes fastest.
Arguments:
- gradients: bfloat16 [16384, 65536], P('run', 'entry'), may hold values from -6 to 6
- probes: bfloat16 [65536, 512], P(('entry', 'run')), may hold values from -0.0234375 to 0.0234375
Outputs:
- projected: float32 [512, 65536], P('run', 'entry')
The draws below stay inside these ranges and needn't reach their ends.
All inputs are finite; a program needn't handle non-finite values.
Results may differ from the reference program's by a relative error of at most 0.0026.
Values may be sent and summed in bfloat16 or wider, within the bound.
No kernel may reach another device: no remote copies, remote signals or barrier semaphores. Data moves between devices by JAX's collectives and lax.ppermute only.
A program may use at most 128 MiB of HBM per device.

```python
import jax
import jax.numpy as jnp
from jax import lax

ENTRIES = 65536
PROBES = 512
RUN_DEV = 512
RUNS = 16384


def levels(own_key, shape, pieces, smallest, high):
    factor_of = 1.0
    for position, shards_of in pieces:
        heights = jax.random.uniform(jax.random.fold_in(jax.random.fold_in(own_key, 6), position), (shards_of,), jnp.float32, smallest / len(pieces), high / len(pieces))
        factor_of = factor_of * jnp.repeat(jnp.exp(heights), shape[position] // shards_of).reshape((-1,) + (1,) * (len(shape) - 1 - position))
    return factor_of


def bell_draw(rng, dims, deviation, limit, cuts=(), kind=jnp.bfloat16):
    entries = jax.random.normal(rng, dims, jnp.float32) * deviation
    if len(cuts) > 0:
        entries = levels(rng, dims, cuts, -0.22, 0.18) * entries
    return jnp.clip(entries, min=-limit, max=limit).astype(kind)


def setup_inputs(seed: int = 0) -> dict:
    arg_keys = jax.random.split(jax.random.key(seed), 3)
    return {
        "gradients": bell_draw(arg_keys[0], (RUNS, ENTRIES), 1.0, 6.0, ((0, 32), (1, 8))),
        "probes": bell_draw(arg_keys[1], (ENTRIES, PROBES), ENTRIES ** -0.5, 0.0234375, ((0, 256),)),
    }


def reference(gradients, probes):
    blocks = gradients.reshape(RUNS // RUN_DEV, RUN_DEV, ENTRIES)

    def sketch_block(block):
        return jnp.dot(block.astype(jnp.float32), probes.astype(jnp.float32), preferred_element_type=jnp.float32)
    sketch = lax.map(sketch_block, blocks).reshape(RUNS, PROBES)
    gram = jnp.dot(sketch.T.astype(jnp.float32), sketch.astype(jnp.float32), precision=lax.Precision.HIGHEST, preferred_element_type=jnp.float32)
    factor = jnp.linalg.cholesky(gram)
    basis = lax.linalg.triangular_solve(factor, sketch, left_side=False, lower=True, transpose_a=True).astype(jnp.bfloat16)
    basis_blocks = basis.reshape(RUNS // RUN_DEV, RUN_DEV, PROBES)

    def project_block(total, pair):
        left, block = pair
        term = lax.dot_general(left.astype(jnp.float32), block.astype(jnp.float32), (((0,), (0,)), ((), ())), preferred_element_type=jnp.float32)
        return (total + term, None)
    start = jnp.zeros((PROBES, ENTRIES), jnp.float32)
    projected, unused = lax.scan(project_block, start, (basis_blocks, blocks))
    return projected
```

```python
import functools

import jax
import jax.numpy as jnp
from jax import lax
from jax.sharding import PartitionSpec as P

HI = lax.Precision.HIGHEST
BLOCK = 128


def _swap(x, axis, size, bit):
    perm = [(i, i ^ (1 << bit)) for i in range(size)]
    return lax.ppermute(x, axis, perm)


def all_reduce(x, axis, size, bits):
    shape = x.shape
    x = x.reshape(-1)
    idx = lax.axis_index(axis)
    for bit in bits:
        mine = (idx >> bit) & 1
        halves = x.reshape(2, -1)
        keep = lax.dynamic_index_in_dim(halves, mine, 0, keepdims=False)
        send = lax.dynamic_index_in_dim(halves, 1 - mine, 0, keepdims=False)
        x = keep + _swap(send, axis, size, bit)
    for bit in reversed(bits):
        mine = (idx >> bit) & 1
        other = _swap(x, axis, size, bit)
        lo = jnp.where(mine == 0, x, other)
        hi = jnp.where(mine == 0, other, x)
        x = jnp.concatenate([lo, hi])
    return x.reshape(shape)


def inverse_factor(gram):
    n = gram.shape[0]
    nb = n // BLOCK
    eye = jnp.eye(BLOCK, dtype=gram.dtype)
    cols = []
    inv_diag = []
    for j in range(nb):
        s = j * BLOCK
        panel = gram[s:, s:s + BLOCK]
        if j > 0:
            left = jnp.concatenate([c[s - k * BLOCK:] for k, c in enumerate(cols)], axis=1)
            top = left[:BLOCK]
            panel = panel - jnp.dot(left, top.T, precision=HI)
        ljj = jnp.linalg.cholesky(panel[:BLOCK])
        ijj = lax.linalg.triangular_solve(ljj, eye, left_side=True, lower=True)
        if j < nb - 1:
            below = jnp.dot(panel[BLOCK:], ijj.T, precision=HI)
            cols.append(jnp.concatenate([ljj, below], axis=0))
        else:
            cols.append(ljj)
        inv_diag.append(ijj)

    def lblock(i, k):
        return cols[k][(i - k) * BLOCK:(i - k + 1) * BLOCK]

    inv = [[None] * nb for _ in range(nb)]
    for i in range(nb):
        inv[i][i] = inv_diag[i]
        for j in range(i - 1, -1, -1):
            acc = jnp.dot(lblock(i, j), inv[j][j], precision=HI)
            for k in range(j + 1, i):
                acc = acc + jnp.dot(lblock(i, k), inv[k][j], precision=HI)
            inv[i][j] = -jnp.dot(inv_diag[i], acc, precision=HI)
    zero = jnp.zeros((BLOCK, BLOCK), gram.dtype)
    rows = [jnp.concatenate([inv[i][j] if j <= i else zero for j in range(nb)], axis=1) for i in range(nb)]
    return jnp.concatenate(rows, axis=0)


def per_device(runs, entries, gradients, probes):
    run_bits = list(range(runs.bit_length() - 1))
    partial_sketch = jnp.dot(
        gradients,
        lax.all_gather(probes, "run", axis=0, tiled=True),
        preferred_element_type=jnp.float32,
    )
    sketch = all_reduce(partial_sketch, "entry", entries, list(range(entries.bit_length() - 1)))
    local_gram = jnp.dot(
        sketch.T, sketch, precision=HI, preferred_element_type=jnp.float32
    )
    gram = all_reduce(local_gram, "run", runs, run_bits)
    inv = inverse_factor(gram)
    basis = jnp.dot(sketch, inv.T, precision=HI).astype(jnp.bfloat16)
    return lax.psum_scatter(
        lax.dot_general(
            basis, gradients, (((0,), (0,)), ((), ())), preferred_element_type=jnp.float32
        ),
        "run",
        scatter_dimension=0,
        tiled=True,
    )


def solution(mesh):
    placed = (P("run", "entry"), P(("entry", "run"), None))
    body = functools.partial(per_device, mesh.shape["run"], mesh.shape["entry"])
    return jax.shard_map(
        body, mesh=mesh, in_specs=placed, out_specs=P("run", "entry"), check_vma=False
    )
```

```python
import functools

import jax
import jax.numpy as jnp
from jax import lax
from jax.sharding import PartitionSpec as P

HI = lax.Precision.HIGHEST
BLOCK = 128


def _swap(x, axis, size, bit):
    perm = [(i, i ^ (1 << bit)) for i in range(size)]
    return lax.ppermute(x, axis, perm)


def all_reduce(x, axis, size, bits):
    shape = x.shape
    x = x.reshape(-1)
    idx = lax.axis_index(axis)
    for bit in bits:
        mine = (idx >> bit) & 1
        halves = x.reshape(2, -1)
        keep = lax.dynamic_index_in_dim(halves, mine, 0, keepdims=False)
        send = lax.dynamic_index_in_dim(halves, 1 - mine, 0, keepdims=False)
        x = keep + _swap(send, axis, size, bit)
    for bit in reversed(bits):
        mine = (idx >> bit) & 1
        other = _swap(x, axis, size, bit)
        lo = jnp.where(mine == 0, x, other)
        hi = jnp.where(mine == 0, other, x)
        x = jnp.concatenate([lo, hi])
    return x.reshape(shape)


def inverse_factor(gram):
    n = gram.shape[0]
    nb = n // BLOCK
    eye = jnp.eye(BLOCK, dtype=gram.dtype)
    cols = []
    inv_diag = []
    for j in range(nb):
        s = j * BLOCK
        panel = gram[s:, s:s + BLOCK]
        if j > 0:
            left = jnp.concatenate([c[s - k * BLOCK:] for k, c in enumerate(cols)], axis=1)
            top = left[:BLOCK]
            panel = panel - jnp.dot(left, top.T, precision=HI)
        ljj = jnp.linalg.cholesky(panel[:BLOCK])
        ijj = lax.linalg.triangular_solve(ljj, eye, left_side=True, lower=True)
        if j < nb - 1:
            below = jnp.dot(panel[BLOCK:], ijj.T, precision=HI)
            cols.append(jnp.concatenate([ljj, below], axis=0))
        else:
            cols.append(ljj)
        inv_diag.append(ijj)

    def lblock(i, k):
        return cols[k][(i - k) * BLOCK:(i - k + 1) * BLOCK]

    inv = [[None] * nb for _ in range(nb)]
    for i in range(nb):
        inv[i][i] = inv_diag[i]
        for j in range(i - 1, -1, -1):
            acc = jnp.dot(lblock(i, j), inv[j][j], precision=HI)
            for k in range(j + 1, i):
                acc = acc + jnp.dot(lblock(i, k), inv[k][j], precision=HI)
            inv[i][j] = -jnp.dot(inv_diag[i], acc, precision=HI)
    zero = jnp.zeros((BLOCK, BLOCK), gram.dtype)
    rows = [jnp.concatenate([inv[i][j] if j <= i else zero for j in range(nb)], axis=1) for i in range(nb)]
    return jnp.concatenate(rows, axis=0)


def per_device(runs, entries, gradients, probes):
    run_bits = list(range(runs.bit_length() - 1))
    partial_sketch = jnp.dot(
        gradients,
        lax.all_gather(probes, "run", axis=0, tiled=True),
        preferred_element_type=jnp.float32,
    )
    sketch = all_reduce(partial_sketch, "entry", entries, list(range(entries.bit_length() - 1)))
    local_gram = jnp.dot(
        sketch.T, sketch, precision=HI, preferred_element_type=jnp.float32
    )
    gram = all_reduce(local_gram, "run", runs, run_bits)
    inv = inverse_factor(gram)
    basis = jnp.dot(sketch, inv.T, precision=HI).astype(jnp.bfloat16)
    return reduce_scatter_projection(basis, gradients, runs)


def reduce_scatter_projection(basis, gradients, runs):
    nz = runs // 4
    probes = basis.shape[1]
    rows = probes // runs
    idx = lax.axis_index("run")
    core = idx % 2
    xlo = (idx // 2) % 2
    z = idx // 4
    cols = basis.reshape(basis.shape[0], nz, 2, 2, rows)

    def project(c):
        b = lax.dynamic_index_in_dim(cols, c, 3, keepdims=False).reshape(basis.shape[0], -1)
        out = lax.dot_general(b, gradients, (((0,), (0,)), ((), ())), preferred_element_type=jnp.float32)
        return out.reshape(nz, 2, rows, gradients.shape[1])

    sent = project(1 - core)
    got = lax.ppermute(sent, "run", [(i, i ^ 1) for i in range(runs)])
    own = project(core)
    half = gradients.shape[1] // 2

    def ring(lo, step_sign):
        perm = [(i, (i + 4 * step_sign) % runs) for i in range(runs)]
        acc = None
        for s in range(nz - 1):
            d = (z - step_sign * (1 + s)) % nz
            part = (lax.dynamic_index_in_dim(own, d, 0, keepdims=False)[..., lo:lo + half]
                    + lax.dynamic_index_in_dim(got, d, 0, keepdims=False)[..., lo:lo + half])
            acc = lax.ppermute(part if acc is None else acc + part, "run", perm)
        part = (lax.dynamic_index_in_dim(own, z, 0, keepdims=False)[..., lo:lo + half]
                + lax.dynamic_index_in_dim(got, z, 0, keepdims=False)[..., lo:lo + half])
        return acc + part

    mine = jnp.concatenate([ring(0, 1), ring(half, -1)], axis=-1)
    keep = lax.dynamic_index_in_dim(mine, xlo, 0, keepdims=False)
    send = lax.dynamic_index_in_dim(mine, 1 - xlo, 0, keepdims=False)
    return keep + lax.ppermute(send, "run", [(i, i ^ 2) for i in range(runs)])


def solution(mesh):
    placed = (P("run", "entry"), P(("entry", "run"), None))
    body = functools.partial(per_device, mesh.shape["run"], mesh.shape["entry"])
    return jax.shard_map(
        body, mesh=mesh, in_specs=placed, out_specs=P("run", "entry"), check_vma=False
    )
```

```python
import functools

import jax
import jax.numpy as jnp
from jax import lax
from jax.sharding import PartitionSpec as P

HI = lax.Precision.HIGHEST
BLOCK = 128


def _swap(x, axis, size, bit):
    perm = [(i, i ^ (1 << bit)) for i in range(size)]
    return lax.ppermute(x, axis, perm)


def all_reduce(x, axis, size, bits):
    shape = x.shape
    blocks = x.reshape(size, -1)
    mine = jnp.sum(lax.all_to_all(blocks, axis, 0, 0), axis=0)
    full = lax.all_to_all(jnp.broadcast_to(mine, blocks.shape), axis, 0, 0)
    return full.reshape(shape)


def inverse_factor(gram):
    n = gram.shape[0]
    nb = n // BLOCK
    eye = jnp.eye(BLOCK, dtype=gram.dtype)
    cols = []
    inv_diag = []
    for j in range(nb):
        s = j * BLOCK
        panel = gram[s:, s:s + BLOCK]
        if j > 0:
            left = jnp.concatenate([c[s - k * BLOCK:] for k, c in enumerate(cols)], axis=1)
            top = left[:BLOCK]
            panel = panel - jnp.dot(left, top.T, precision=HI)
        ljj = jnp.linalg.cholesky(panel[:BLOCK])
        ijj = lax.linalg.triangular_solve(ljj, eye, left_side=True, lower=True)
        if j < nb - 1:
            below = jnp.dot(panel[BLOCK:], ijj.T, precision=HI)
            cols.append(jnp.concatenate([ljj, below], axis=0))
        else:
            cols.append(ljj)
        inv_diag.append(ijj)

    def lblock(i, k):
        return cols[k][(i - k) * BLOCK:(i - k + 1) * BLOCK]

    inv = [[None] * nb for _ in range(nb)]
    for i in range(nb):
        inv[i][i] = inv_diag[i]
        for j in range(i - 1, -1, -1):
            acc = jnp.dot(lblock(i, j), inv[j][j], precision=HI)
            for k in range(j + 1, i):
                acc = acc + jnp.dot(lblock(i, k), inv[k][j], precision=HI)
            inv[i][j] = -jnp.dot(inv_diag[i], acc, precision=HI)
    zero = jnp.zeros((BLOCK, BLOCK), gram.dtype)
    rows = [jnp.concatenate([inv[i][j] if j <= i else zero for j in range(nb)], axis=1) for i in range(nb)]
    return jnp.concatenate(rows, axis=0)


def per_device(runs, entries, gradients, probes):
    run_bits = list(range(runs.bit_length() - 1))
    partial_sketch = jnp.dot(
        gradients,
        lax.all_gather(probes, "run", axis=0, tiled=True),
        preferred_element_type=jnp.float32,
    )
    sketch = all_reduce(partial_sketch, "entry", entries, list(range(entries.bit_length() - 1)))
    local_gram = jnp.dot(
        sketch.T, sketch, precision=HI, preferred_element_type=jnp.float32
    )
    gram = all_reduce(local_gram, "run", runs, run_bits)
    inv = inverse_factor(gram)
    basis = jnp.dot(sketch, inv.T, precision=HI).astype(jnp.bfloat16)
    return reduce_scatter_projection(basis, gradients, runs)


def reduce_scatter_projection(basis, gradients, runs):
    nz = runs // 4
    probes = basis.shape[1]
    rows = probes // runs
    idx = lax.axis_index("run")
    core = idx % 2
    xlo = (idx // 2) % 2
    z = idx // 4
    cols = basis.reshape(basis.shape[0], nz, 2, 2, rows)

    def project(c):
        b = lax.dynamic_index_in_dim(cols, c, 3, keepdims=False).reshape(basis.shape[0], -1)
        out = lax.dot_general(b, gradients, (((0,), (0,)), ((), ())), preferred_element_type=jnp.float32)
        return out.reshape(nz, 2, rows, gradients.shape[1])

    sent = project(1 - core)
    got = lax.ppermute(sent, "run", [(i, i ^ 1) for i in range(runs)])
    own = project(core)

    def ring(x, step_sign):
        perm = [(i, (i + 4 * step_sign) % runs) for i in range(runs)]

        def part(d):
            return own[d, x] + got[d, x]

        acc = None
        for s in range(nz - 1):
            d = (z - step_sign * (1 + s)) % nz
            acc = lax.ppermute(part(d) if acc is None else acc + part(d), "run", perm)
        return acc + part(z)

    lo, hi = ring(0, 1), ring(1, -1)
    keep = jnp.where(xlo == 0, lo, hi)
    send = jnp.where(xlo == 0, hi, lo)
    return keep + lax.ppermute(send, "run", [(i, i ^ 2) for i in range(runs)])


def solution(mesh):
    placed = (P("run", "entry"), P(("entry", "run"), None))
    body = functools.partial(per_device, mesh.shape["run"], mesh.shape["entry"])
    return jax.shard_map(
        body, mesh=mesh, in_specs=placed, out_specs=P("run", "entry"), check_vma=False
    )
```

```python
import functools

import jax
import jax.numpy as jnp
from jax import lax
from jax.sharding import PartitionSpec as P

HI = lax.Precision.HIGHEST
BLOCK = 128


def _swap(x, axis, size, bit):
    perm = [(i, i ^ (1 << bit)) for i in range(size)]
    return lax.ppermute(x, axis, perm)


def all_reduce_halving(x, axis, size, bits):
    shape = x.shape
    x = x.reshape(-1)
    idx = lax.axis_index(axis)
    for bit in bits:
        mine = (idx >> bit) & 1
        halves = x.reshape(2, -1)
        keep = lax.dynamic_index_in_dim(halves, mine, 0, keepdims=False)
        send = lax.dynamic_index_in_dim(halves, 1 - mine, 0, keepdims=False)
        x = keep + _swap(send, axis, size, bit)
    for bit in reversed(bits):
        mine = (idx >> bit) & 1
        other = _swap(x, axis, size, bit)
        lo = jnp.where(mine == 0, x, other)
        hi = jnp.where(mine == 0, other, x)
        x = jnp.concatenate([lo, hi])
    return x.reshape(shape)


def all_reduce_a2a(x, axis, size):
    shape = x.shape
    blocks = x.reshape(size, -1)
    mine = jnp.sum(lax.all_to_all(blocks, axis, 0, 0), axis=0)
    full = lax.all_to_all(jnp.broadcast_to(mine, blocks.shape), axis, 0, 0)
    return full.reshape(shape)


def inverse_factor(gram):
    n = gram.shape[0]
    nb = n // BLOCK
    eye = jnp.eye(BLOCK, dtype=gram.dtype)
    cols = []
    inv_diag = []
    for j in range(nb):
        s = j * BLOCK
        panel = gram[s:, s:s + BLOCK]
        if j > 0:
            left = jnp.concatenate([c[s - k * BLOCK:] for k, c in enumerate(cols)], axis=1)
            top = left[:BLOCK]
            panel = panel - jnp.dot(left, top.T, precision=HI)
        ljj = jnp.linalg.cholesky(panel[:BLOCK])
        ijj = lax.linalg.triangular_solve(ljj, eye, left_side=True, lower=True)
        if j < nb - 1:
            below = jnp.dot(panel[BLOCK:], ijj.T, precision=HI)
            cols.append(jnp.concatenate([ljj, below], axis=0))
        else:
            cols.append(ljj)
        inv_diag.append(ijj)

    def lblock(i, k):
        return cols[k][(i - k) * BLOCK:(i - k + 1) * BLOCK]

    inv = [[None] * nb for _ in range(nb)]
    for i in range(nb):
        inv[i][i] = inv_diag[i]
        for j in range(i - 1, -1, -1):
            acc = jnp.dot(lblock(i, j), inv[j][j], precision=HI)
            for k in range(j + 1, i):
                acc = acc + jnp.dot(lblock(i, k), inv[k][j], precision=HI)
            inv[i][j] = -jnp.dot(inv_diag[i], acc, precision=HI)
    zero = jnp.zeros((BLOCK, BLOCK), gram.dtype)
    rows = [jnp.concatenate([inv[i][j] if j <= i else zero for j in range(nb)], axis=1) for i in range(nb)]
    return jnp.concatenate(rows, axis=0)


def per_device(runs, entries, gradients, probes):
    run_bits = list(range(runs.bit_length() - 1))
    partial_sketch = jnp.dot(
        gradients,
        lax.all_gather(probes, "run", axis=0, tiled=True),
        preferred_element_type=jnp.float32,
    )
    sketch = all_reduce_a2a(partial_sketch, "entry", entries)
    local_gram = jnp.dot(
        sketch.T, sketch, precision=HI, preferred_element_type=jnp.float32
    )
    gram = all_reduce_halving(local_gram, "run", runs, run_bits)
    inv = inverse_factor(gram)
    basis = jnp.dot(sketch, inv.T, precision=HI).astype(jnp.bfloat16)
    return reduce_scatter_projection(basis, gradients, runs)


def reduce_scatter_projection(basis, gradients, runs):
    nz = runs // 4
    probes = basis.shape[1]
    rows = probes // runs
    idx = lax.axis_index("run")
    core = idx % 2
    xlo = (idx // 2) % 2
    z = idx // 4
    cols = basis.reshape(basis.shape[0], nz, 2, 2, rows)

    def project(c):
        b = lax.dynamic_index_in_dim(cols, c, 3, keepdims=False).reshape(basis.shape[0], -1)
        out = lax.dot_general(b, gradients, (((0,), (0,)), ((), ())), preferred_element_type=jnp.float32)
        return out.reshape(nz, 2, rows, gradients.shape[1])

    sent = project(1 - core)
    got = lax.ppermute(sent, "run", [(i, i ^ 1) for i in range(runs)])
    own = project(core)

    split = rows // 2

    def ring(x, r0, step_sign):
        perm = [(i, (i + 4 * step_sign) % runs) for i in range(runs)]

        def part(d):
            return own[d, x, r0:r0 + split] + got[d, x, r0:r0 + split]

        acc = None
        for s in range(nz - 1):
            d = (z - step_sign * (1 + s)) % nz
            acc = lax.ppermute(part(d) if acc is None else acc + part(d), "run", perm)
        return acc + part(z)

    lo = jnp.concatenate([ring(0, 0, 1), ring(0, split, 1)], axis=0)
    hi = jnp.concatenate([ring(1, 0, -1), ring(1, split, -1)], axis=0)
    keep = jnp.where(xlo == 0, lo, hi)
    send = jnp.where(xlo == 0, hi, lo)
    return keep + lax.ppermute(send, "run", [(i, i ^ 2) for i in range(runs)])


def solution(mesh):
    placed = (P("run", "entry"), P(("entry", "run"), None))
    body = functools.partial(per_device, mesh.shape["run"], mesh.shape["entry"])
    return jax.shard_map(
        body, mesh=mesh, in_specs=placed, out_specs=P("run", "entry"), check_vma=False
    )
```

```python
import functools

import jax
import jax.numpy as jnp
from jax import lax
from jax.sharding import PartitionSpec as P

HI = lax.Precision.HIGHEST
RUN = ("z", "xlo", "core")
ENTRY = ("xhi", "y")
BLOCK = 128


def _swap(x, axis, size, bit):
    perm = [(i, i ^ (1 << bit)) for i in range(size)]
    return lax.ppermute(x, axis, perm)


def all_reduce_halving(x, axis, size, bits):
    shape = x.shape
    x = x.reshape(-1)
    idx = lax.axis_index(axis)
    for bit in bits:
        mine = (idx >> bit) & 1
        halves = x.reshape(2, -1)
        keep = lax.dynamic_index_in_dim(halves, mine, 0, keepdims=False)
        send = lax.dynamic_index_in_dim(halves, 1 - mine, 0, keepdims=False)
        x = keep + _swap(send, axis, size, bit)
    for bit in reversed(bits):
        mine = (idx >> bit) & 1
        other = _swap(x, axis, size, bit)
        lo = jnp.where(mine == 0, x, other)
        hi = jnp.where(mine == 0, other, x)
        x = jnp.concatenate([lo, hi])
    return x.reshape(shape)


def all_reduce_a2a(x, axis, size):
    shape = x.shape
    blocks = x.reshape(size, -1)
    mine = jnp.sum(lax.all_to_all(blocks, axis, 0, 0), axis=0)
    full = lax.all_to_all(jnp.broadcast_to(mine, blocks.shape), axis, 0, 0)
    return full.reshape(shape)


def inverse_factor(gram):
    n = gram.shape[0]
    nb = n // BLOCK
    eye = jnp.eye(BLOCK, dtype=gram.dtype)
    cols = []
    inv_diag = []
    for j in range(nb):
        s = j * BLOCK
        panel = gram[s:, s:s + BLOCK]
        if j > 0:
            left = jnp.concatenate([c[s - k * BLOCK:] for k, c in enumerate(cols)], axis=1)
            top = left[:BLOCK]
            panel = panel - jnp.dot(left, top.T, precision=HI)
        ljj = jnp.linalg.cholesky(panel[:BLOCK])
        ijj = lax.linalg.triangular_solve(ljj, eye, left_side=True, lower=True)
        if j < nb - 1:
            below = jnp.dot(panel[BLOCK:], ijj.T, precision=HI)
            cols.append(jnp.concatenate([ljj, below], axis=0))
        else:
            cols.append(ljj)
        inv_diag.append(ijj)

    def lblock(i, k):
        return cols[k][(i - k) * BLOCK:(i - k + 1) * BLOCK]

    inv = [[None] * nb for _ in range(nb)]
    for i in range(nb):
        inv[i][i] = inv_diag[i]
        for j in range(i - 1, -1, -1):
            acc = jnp.dot(lblock(i, j), inv[j][j], precision=HI)
            for k in range(j + 1, i):
                acc = acc + jnp.dot(lblock(i, k), inv[k][j], precision=HI)
            inv[i][j] = -jnp.dot(inv_diag[i], acc, precision=HI)
    zero = jnp.zeros((BLOCK, BLOCK), gram.dtype)
    rows = [jnp.concatenate([inv[i][j] if j <= i else zero for j in range(nb)], axis=1) for i in range(nb)]
    return jnp.concatenate(rows, axis=0)


def gathered_sketch(gradients, probes, runs):
    nz = runs // 4
    z = lax.axis_index("z")
    xlo = lax.axis_index("xlo")
    core = lax.axis_index("core")
    pair = [(0, 1), (1, 0)]
    other = lax.ppermute(probes, "xlo", pair)
    by_xlo = jnp.stack([jnp.where(xlo == 0, probes, other), jnp.where(xlo == 0, other, probes)])
    other = lax.ppermute(by_xlo, "core", pair)
    chip = jnp.stack([jnp.where(core == 0, by_xlo, other), jnp.where(core == 0, other, by_xlo)], axis=1)
    chip = chip.reshape(2, 2 * probes.shape[0], probes.shape[1])
    half = lax.dynamic_index_in_dim(chip, core, 0, keepdims=False)

    def hops(step, count):
        perm = [(r, ((r // 4 + step) % nz) * 4 + r % 4) for r in range(runs)]
        out, cur = [], half
        for _ in range(count):
            cur = lax.ppermute(cur, RUN, perm)
            out.append(cur)
        return out

    ahead, behind = hops(1, nz // 2), hops(-1, (nz - 1) // 2)
    mine = [half] + ahead + behind
    where_from = [z] + [(z - k) % nz for k in range(1, len(ahead) + 1)] + [(z + k) % nz for k in range(1, len(behind) + 1)]
    theirs = lax.ppermute(jnp.stack(mine), "core", pair)
    full = jnp.zeros((nz,) + chip.shape, chip.dtype)
    zero = jnp.zeros((), z.dtype)
    for j, zi in enumerate(where_from):
        full = lax.dynamic_update_slice(full, mine[j][None, None], (zi, core, zero, zero))
        full = lax.dynamic_update_slice(full, theirs[j][None, None], (zi, 1 - core, zero, zero))
    return jnp.dot(gradients, full.reshape(-1, probes.shape[1]), preferred_element_type=jnp.float32)


def per_device(runs, entries, gradients, probes):
    run_bits = list(range(runs.bit_length() - 1))
    partial_sketch = gathered_sketch(gradients, probes, runs)
    sketch = all_reduce_a2a(partial_sketch, ENTRY, entries)
    local_gram = jnp.dot(
        sketch.T, sketch, precision=HI, preferred_element_type=jnp.float32
    )
    gram = all_reduce_halving(local_gram, RUN, runs, run_bits)
    inv = inverse_factor(gram)
    basis = jnp.dot(sketch, inv.T, precision=HI).astype(jnp.bfloat16)
    return reduce_scatter_projection(basis, gradients, runs)


def reduce_scatter_projection(basis, gradients, runs):
    nz = runs // 4
    probes = basis.shape[1]
    rows = probes // runs
    idx = lax.axis_index(RUN)
    core = idx % 2
    xlo = (idx // 2) % 2
    z = idx // 4
    cols = basis.reshape(basis.shape[0], nz, 2, 2, rows)

    def project(c):
        b = lax.dynamic_index_in_dim(cols, c, 3, keepdims=False).reshape(basis.shape[0], -1)
        out = lax.dot_general(b, gradients, (((0,), (0,)), ((), ())), preferred_element_type=jnp.float32)
        return out.reshape(nz, 2, rows, gradients.shape[1])

    sent = project(1 - core)
    got = lax.ppermute(sent, RUN, [(i, i ^ 1) for i in range(runs)])
    own = project(core)

    split = rows // 2

    def ring(x, r0, step_sign):
        perm = [(i, (i + 4 * step_sign) % runs) for i in range(runs)]

        def part(d):
            return own[d, x, r0:r0 + split] + got[d, x, r0:r0 + split]

        acc = None
        for s in range(nz - 1):
            d = (z - step_sign * (1 + s)) % nz
            acc = lax.ppermute(part(d) if acc is None else acc + part(d), RUN, perm)
        return acc + part(z)

    lo = jnp.concatenate([ring(0, 0, 1), ring(0, split, 1)], axis=0)
    hi = jnp.concatenate([ring(1, 0, -1), ring(1, split, -1)], axis=0)
    keep = jnp.where(xlo == 0, lo, hi)
    send = jnp.where(xlo == 0, hi, lo)
    return keep + lax.ppermute(send, RUN, [(i, i ^ 2) for i in range(runs)])


def solution(mesh):
    runs, entries = mesh.shape["run"], mesh.shape["entry"]
    split = jax.sharding.Mesh(mesh.devices.reshape(runs // 4, 2, 2, 2, entries // 2), RUN + ENTRY)
    placed = (P(RUN, ENTRY), P(ENTRY + RUN, None))
    body = functools.partial(per_device, runs, entries)
    return jax.shard_map(
        body, mesh=split, in_specs=placed, out_specs=P(RUN, ENTRY), check_vma=False
    )
```

```python
import functools

import jax
import jax.numpy as jnp
from jax import lax
from jax.sharding import PartitionSpec as P

HI = lax.Precision.HIGHEST
RUN = ("z", "xlo", "core")
ENTRY = ("xhi", "y")
BLOCK = 128


def _swap(x, axis, size, bit):
    perm = [(i, i ^ (1 << bit)) for i in range(size)]
    return lax.ppermute(x, axis, perm)


def all_reduce_halving(x, axis, size, bits):
    shape = x.shape
    x = x.reshape(-1)
    idx = lax.axis_index(axis)
    for bit in bits:
        mine = (idx >> bit) & 1
        halves = x.reshape(2, -1)
        keep = lax.dynamic_index_in_dim(halves, mine, 0, keepdims=False)
        send = lax.dynamic_index_in_dim(halves, 1 - mine, 0, keepdims=False)
        x = keep + _swap(send, axis, size, bit)
    for bit in reversed(bits):
        mine = (idx >> bit) & 1
        other = _swap(x, axis, size, bit)
        lo = jnp.where(mine == 0, x, other)
        hi = jnp.where(mine == 0, other, x)
        x = jnp.concatenate([lo, hi])
    return x.reshape(shape)


def all_reduce_a2a(x, axis, size):
    shape = x.shape
    blocks = x.reshape(size, -1)
    mine = jnp.sum(lax.all_to_all(blocks, axis, 0, 0), axis=0)
    full = lax.all_to_all(jnp.broadcast_to(mine, blocks.shape), axis, 0, 0)
    return full.reshape(shape)


def inverse_factor(gram):
    n = gram.shape[0]
    nb = n // BLOCK
    eye = jnp.eye(BLOCK, dtype=gram.dtype)
    cols = []
    inv_diag = []
    for j in range(nb):
        s = j * BLOCK
        panel = gram[s:, s:s + BLOCK]
        if j > 0:
            left = jnp.concatenate([c[s - k * BLOCK:] for k, c in enumerate(cols)], axis=1)
            top = left[:BLOCK]
            panel = panel - jnp.dot(left, top.T, precision=HI)
        ljj = lax.linalg.cholesky(panel[:BLOCK], symmetrize_input=False)
        ijj = lax.linalg.triangular_solve(ljj, eye, left_side=True, lower=True)
        if j < nb - 1:
            below = jnp.dot(panel[BLOCK:], ijj.T, precision=HI)
            cols.append(jnp.concatenate([ljj, below], axis=0))
        else:
            cols.append(ljj)
        inv_diag.append(ijj)

    def lblock(i, k):
        return cols[k][(i - k) * BLOCK:(i - k + 1) * BLOCK]

    inv = [[None] * nb for _ in range(nb)]
    for i in range(nb):
        inv[i][i] = inv_diag[i]
        for j in range(i - 1, -1, -1):
            acc = jnp.dot(lblock(i, j), inv[j][j], precision=HI)
            for k in range(j + 1, i):
                acc = acc + jnp.dot(lblock(i, k), inv[k][j], precision=HI)
            inv[i][j] = -jnp.dot(inv_diag[i], acc, precision=HI)
    zero = jnp.zeros((BLOCK, BLOCK), gram.dtype)
    rows = [jnp.concatenate([inv[i][j] if j <= i else zero for j in range(nb)], axis=1) for i in range(nb)]
    return jnp.concatenate(rows, axis=0)


def gathered_sketch(gradients, probes, runs):
    nz = runs // 4
    z = lax.axis_index("z")
    xlo = lax.axis_index("xlo")
    core = lax.axis_index("core")
    pair = [(0, 1), (1, 0)]
    other = lax.ppermute(probes, "xlo", pair)
    by_xlo = jnp.stack([jnp.where(xlo == 0, probes, other), jnp.where(xlo == 0, other, probes)])
    other = lax.ppermute(by_xlo, "core", pair)
    chip = jnp.stack([jnp.where(core == 0, by_xlo, other), jnp.where(core == 0, other, by_xlo)], axis=1)
    chip = chip.reshape(2, 2 * probes.shape[0], probes.shape[1])
    half = lax.dynamic_index_in_dim(chip, core, 0, keepdims=False)

    def hops(step, count):
        perm = [(r, ((r // 4 + step) % nz) * 4 + r % 4) for r in range(runs)]
        out, cur = [], half
        for _ in range(count):
            cur = lax.ppermute(cur, RUN, perm)
            out.append(cur)
        return out

    ahead, behind = hops(1, nz // 2), hops(-1, (nz - 1) // 2)
    mine = [half] + ahead + behind
    where_from = [z] + [(z - k) % nz for k in range(1, len(ahead) + 1)] + [(z + k) % nz for k in range(1, len(behind) + 1)]
    theirs = lax.ppermute(jnp.stack(mine), "core", pair)
    full = jnp.zeros((nz,) + chip.shape, chip.dtype)
    zero = jnp.zeros((), z.dtype)
    for j, zi in enumerate(where_from):
        full = lax.dynamic_update_slice(full, mine[j][None, None], (zi, core, zero, zero))
        full = lax.dynamic_update_slice(full, theirs[j][None, None], (zi, 1 - core, zero, zero))
    return jnp.dot(gradients, full.reshape(-1, probes.shape[1]), preferred_element_type=jnp.float32)


def per_device(runs, entries, gradients, probes):
    run_bits = list(range(runs.bit_length() - 1))
    partial_sketch = gathered_sketch(gradients, probes, runs)
    sketch = all_reduce_a2a(partial_sketch, ENTRY, entries)
    local_gram = jnp.dot(
        sketch.T, sketch, precision=HI, preferred_element_type=jnp.float32
    )
    gram = all_reduce_halving(local_gram, RUN, runs, run_bits)
    inv = inverse_factor(gram)
    basis = jnp.dot(sketch, inv.T, precision=HI).astype(jnp.bfloat16)
    return reduce_scatter_projection(basis, gradients, runs)


def reduce_scatter_projection(basis, gradients, runs):
    nz = runs // 4
    probes = basis.shape[1]
    rows = probes // runs
    idx = lax.axis_index(RUN)
    core = idx % 2
    xlo = (idx // 2) % 2
    z = idx // 4
    cols = basis.reshape(basis.shape[0], nz, 2, 2, rows)

    def project(c):
        b = lax.dynamic_index_in_dim(cols, c, 3, keepdims=False).reshape(basis.shape[0], -1)
        out = lax.dot_general(b, gradients, (((0,), (0,)), ((), ())), preferred_element_type=jnp.float32)
        return out.reshape(nz, 2, rows, gradients.shape[1])

    sent = project(1 - core)
    got = lax.ppermute(sent, RUN, [(i, i ^ 1) for i in range(runs)])
    own = project(core)

    split = rows // 2

    def ring(x, r0, step_sign):
        perm = [(i, (i + 4 * step_sign) % runs) for i in range(runs)]

        def part(d):
            return own[d, x, r0:r0 + split] + got[d, x, r0:r0 + split]

        acc = None
        for s in range(nz - 1):
            d = (z - step_sign * (1 + s)) % nz
            acc = lax.ppermute(part(d) if acc is None else acc + part(d), RUN, perm)
        return acc + part(z)

    lo = jnp.concatenate([ring(0, 0, 1), ring(0, split, 1)], axis=0)
    hi = jnp.concatenate([ring(1, 0, -1), ring(1, split, -1)], axis=0)
    keep = jnp.where(xlo == 0, lo, hi)
    send = jnp.where(xlo == 0, hi, lo)
    return keep + lax.ppermute(send, RUN, [(i, i ^ 2) for i in range(runs)])


def solution(mesh):
    runs, entries = mesh.shape["run"], mesh.shape["entry"]
    split = jax.sharding.Mesh(mesh.devices.reshape(runs // 4, 2, 2, 2, entries // 2), RUN + ENTRY)
    placed = (P(RUN, ENTRY), P(ENTRY + RUN, None))
    body = functools.partial(per_device, runs, entries)
    return jax.shard_map(
        body, mesh=split, in_specs=placed, out_specs=P(RUN, ENTRY), check_vma=False
    )
```

```python
import functools

import jax
import jax.numpy as jnp
from jax import lax
from jax.sharding import PartitionSpec as P

HI = lax.Precision.HIGHEST
RUN = ("z", "xlo", "core")
ENTRY = ("xhi", "y")
BLOCK = 128


def _swap(x, axis, size, bit):
    perm = [(i, i ^ (1 << bit)) for i in range(size)]
    return lax.ppermute(x, axis, perm)


def all_reduce_halving(x, axis, size, bits, inner=None, inner_size=1):
    shape = x.shape
    x = x.reshape(-1)
    idx = lax.axis_index(axis)
    for bit in bits:
        mine = (idx >> bit) & 1
        halves = x.reshape(2, -1)
        keep = lax.dynamic_index_in_dim(halves, mine, 0, keepdims=False)
        send = lax.dynamic_index_in_dim(halves, 1 - mine, 0, keepdims=False)
        x = keep + _swap(send, axis, size, bit)
    if inner is not None:
        x = all_reduce_a2a(x, inner, inner_size)
    for bit in reversed(bits):
        mine = (idx >> bit) & 1
        other = _swap(x, axis, size, bit)
        lo = jnp.where(mine == 0, x, other)
        hi = jnp.where(mine == 0, other, x)
        x = jnp.concatenate([lo, hi])
    return x.reshape(shape)


def all_reduce_a2a(x, axis, size):
    shape = x.shape
    blocks = x.reshape(size, -1)
    mine = jnp.sum(lax.all_to_all(blocks, axis, 0, 0), axis=0)
    full = lax.all_to_all(jnp.broadcast_to(mine, blocks.shape), axis, 0, 0)
    return full.reshape(shape)


def inverse_factor(gram):
    n = gram.shape[0]
    nb = n // BLOCK
    eye = jnp.eye(BLOCK, dtype=gram.dtype)
    cols = []
    inv_diag = []
    for j in range(nb):
        s = j * BLOCK
        panel = gram[s:, s:s + BLOCK]
        if j > 0:
            left = jnp.concatenate([c[s - k * BLOCK:] for k, c in enumerate(cols)], axis=1)
            top = left[:BLOCK]
            panel = panel - jnp.dot(left, top.T, precision=HI)
        ljj = lax.linalg.cholesky(panel[:BLOCK], symmetrize_input=False)
        ijj = lax.linalg.triangular_solve(ljj, eye, left_side=True, lower=True)
        if j < nb - 1:
            below = jnp.dot(panel[BLOCK:], ijj.T, precision=HI)
            cols.append(jnp.concatenate([ljj, below], axis=0))
        else:
            cols.append(ljj)
        inv_diag.append(ijj)

    def lblock(i, k):
        return cols[k][(i - k) * BLOCK:(i - k + 1) * BLOCK]

    inv = [[None] * nb for _ in range(nb)]
    for i in range(nb):
        inv[i][i] = inv_diag[i]
        for j in range(i - 1, -1, -1):
            acc = jnp.dot(lblock(i, j), inv[j][j], precision=HI)
            for k in range(j + 1, i):
                acc = acc + jnp.dot(lblock(i, k), inv[k][j], precision=HI)
            inv[i][j] = -jnp.dot(inv_diag[i], acc, precision=HI)
    zero = jnp.zeros((BLOCK, BLOCK), gram.dtype)
    rows = [jnp.concatenate([inv[i][j] if j <= i else zero for j in range(nb)], axis=1) for i in range(nb)]
    return jnp.concatenate(rows, axis=0)


def gathered_sketch(gradients, probes, runs):
    nz = runs // 4
    z = lax.axis_index("z")
    xlo = lax.axis_index("xlo")
    core = lax.axis_index("core")
    pair = [(0, 1), (1, 0)]
    other = lax.ppermute(probes, "xlo", pair)
    by_xlo = jnp.stack([jnp.where(xlo == 0, probes, other), jnp.where(xlo == 0, other, probes)])
    other = lax.ppermute(by_xlo, "core", pair)
    chip = jnp.stack([jnp.where(core == 0, by_xlo, other), jnp.where(core == 0, other, by_xlo)], axis=1)
    chip = chip.reshape(2, 2 * probes.shape[0], probes.shape[1])
    half = lax.dynamic_index_in_dim(chip, core, 0, keepdims=False)

    def hops(step, count):
        perm = [(r, ((r // 4 + step) % nz) * 4 + r % 4) for r in range(runs)]
        out, cur = [], half
        for _ in range(count):
            cur = lax.ppermute(cur, RUN, perm)
            out.append(cur)
        return out

    ahead, behind = hops(1, nz // 2), hops(-1, (nz - 1) // 2)
    mine = [half] + ahead + behind
    where_from = [z] + [(z - k) % nz for k in range(1, len(ahead) + 1)] + [(z + k) % nz for k in range(1, len(behind) + 1)]
    theirs = lax.ppermute(jnp.stack(mine), "core", pair)
    full = jnp.zeros((nz,) + chip.shape, chip.dtype)
    zero = jnp.zeros((), z.dtype)
    for j, zi in enumerate(where_from):
        full = lax.dynamic_update_slice(full, mine[j][None, None], (zi, core, zero, zero))
        full = lax.dynamic_update_slice(full, theirs[j][None, None], (zi, 1 - core, zero, zero))
    return jnp.dot(gradients, full.reshape(-1, probes.shape[1]), preferred_element_type=jnp.float32)


def per_device(runs, entries, gradients, probes):
    run_bits = list(range(runs.bit_length() - 1))
    partial_sketch = gathered_sketch(gradients, probes, runs)
    sketch = all_reduce_a2a(partial_sketch, ENTRY, entries)
    local_gram = jnp.dot(
        sketch.T, sketch, precision=HI, preferred_element_type=jnp.float32
    )
    gram = all_reduce_halving(local_gram, RUN, runs, [0, 1], "z", runs // 4)
    inv = inverse_factor(gram)
    basis = jnp.dot(sketch, inv.T, precision=HI).astype(jnp.bfloat16)
    return reduce_scatter_projection(basis, gradients, runs)


def reduce_scatter_projection(basis, gradients, runs):
    nz = runs // 4
    probes = basis.shape[1]
    rows = probes // runs
    idx = lax.axis_index(RUN)
    core = idx % 2
    xlo = (idx // 2) % 2
    z = idx // 4
    cols = basis.reshape(basis.shape[0], nz, 2, 2, rows)

    def project(c):
        b = lax.dynamic_index_in_dim(cols, c, 3, keepdims=False).reshape(basis.shape[0], -1)
        out = lax.dot_general(b, gradients, (((0,), (0,)), ((), ())), preferred_element_type=jnp.float32)
        return out.reshape(nz, 2, rows, gradients.shape[1])

    sent = project(1 - core)
    got = lax.ppermute(sent, RUN, [(i, i ^ 1) for i in range(runs)])
    own = project(core)

    split = rows // 2

    def ring(x, r0, step_sign):
        perm = [(i, (i + 4 * step_sign) % runs) for i in range(runs)]

        def part(d):
            return own[d, x, r0:r0 + split] + got[d, x, r0:r0 + split]

        acc = None
        for s in range(nz - 1):
            d = (z - step_sign * (1 + s)) % nz
            acc = lax.ppermute(part(d) if acc is None else acc + part(d), RUN, perm)
        return acc + part(z)

    lo = jnp.concatenate([ring(0, 0, 1), ring(0, split, 1)], axis=0)
    hi = jnp.concatenate([ring(1, 0, -1), ring(1, split, -1)], axis=0)
    keep = jnp.where(xlo == 0, lo, hi)
    send = jnp.where(xlo == 0, hi, lo)
    return keep + lax.ppermute(send, RUN, [(i, i ^ 2) for i in range(runs)])


def solution(mesh):
    runs, entries = mesh.shape["run"], mesh.shape["entry"]
    split = jax.sharding.Mesh(mesh.devices.reshape(runs // 4, 2, 2, 2, entries // 2), RUN + ENTRY)
    placed = (P(RUN, ENTRY), P(ENTRY + RUN, None))
    body = functools.partial(per_device, runs, entries)
    return jax.shard_map(
        body, mesh=split, in_specs=placed, out_specs=P(RUN, ENTRY), check_vma=False
    )
```

```python
import functools

import jax
import jax.numpy as jnp
from jax import lax
from jax.sharding import PartitionSpec as P

HI = lax.Precision.HIGHEST
RUN = ("z", "xlo", "core")
ENTRY = ("xhi", "y")
BLOCK = 128


def _swap(x, axis, size, bit):
    perm = [(i, i ^ (1 << bit)) for i in range(size)]
    return lax.ppermute(x, axis, perm)


def all_reduce_halving(x, axis, size, bits, inner=None, inner_size=1):
    shape = x.shape
    x = x.reshape(-1)
    idx = lax.axis_index(axis)
    for bit in bits:
        mine = (idx >> bit) & 1
        halves = x.reshape(2, -1)
        keep = lax.dynamic_index_in_dim(halves, mine, 0, keepdims=False)
        send = lax.dynamic_index_in_dim(halves, 1 - mine, 0, keepdims=False)
        x = keep + _swap(send, axis, size, bit)
    if inner is not None:
        x = all_reduce_a2a(x, inner, inner_size)
    for bit in reversed(bits):
        mine = (idx >> bit) & 1
        other = _swap(x, axis, size, bit)
        lo = jnp.where(mine == 0, x, other)
        hi = jnp.where(mine == 0, other, x)
        x = jnp.concatenate([lo, hi])
    return x.reshape(shape)


def all_reduce_a2a(x, axis, size):
    shape = x.shape
    blocks = x.reshape(size, -1)
    mine = jnp.sum(lax.all_to_all(blocks, axis, 0, 0), axis=0)
    full = lax.all_to_all(jnp.broadcast_to(mine, blocks.shape), axis, 0, 0)
    return full.reshape(shape)


def inverse_factor(gram):
    n = gram.shape[0]
    nb = n // BLOCK
    eye = jnp.eye(BLOCK, dtype=gram.dtype)
    cols = []
    inv_diag = []
    for j in range(nb):
        s = j * BLOCK
        panel = gram[s:, s:s + BLOCK]
        if j > 0:
            left = jnp.concatenate([c[s - k * BLOCK:] for k, c in enumerate(cols)], axis=1)
            top = left[:BLOCK]
            panel = panel - jnp.dot(left, top.T, precision=HI)
        ljj = lax.linalg.cholesky(panel[:BLOCK], symmetrize_input=False)
        ijj = lax.linalg.triangular_solve(ljj, eye, left_side=True, lower=True)
        if j < nb - 1:
            below = jnp.dot(panel[BLOCK:], ijj.T, precision=HI)
            cols.append(jnp.concatenate([ljj, below], axis=0))
        else:
            cols.append(ljj)
        inv_diag.append(ijj)

    def lblock(i, k):
        return cols[k][(i - k) * BLOCK:(i - k + 1) * BLOCK]

    inv = [[None] * nb for _ in range(nb)]
    for i in range(nb):
        inv[i][i] = inv_diag[i]
        for j in range(i - 1, -1, -1):
            acc = jnp.dot(lblock(i, j), inv[j][j], precision=HI)
            for k in range(j + 1, i):
                acc = acc + jnp.dot(lblock(i, k), inv[k][j], precision=HI)
            inv[i][j] = -jnp.dot(inv_diag[i], acc, precision=HI)
    zero = jnp.zeros((BLOCK, BLOCK), gram.dtype)
    rows = [jnp.concatenate([inv[i][j] if j <= i else zero for j in range(nb)], axis=1) for i in range(nb)]
    return jnp.concatenate(rows, axis=0)


def gathered_sketch(gradients, probes, runs):
    nz = runs // 4
    z = lax.axis_index("z")
    xlo = lax.axis_index("xlo")
    core = lax.axis_index("core")
    pair = [(0, 1), (1, 0)]
    other = lax.ppermute(probes, "xlo", pair)
    by_xlo = jnp.stack([jnp.where(xlo == 0, probes, other), jnp.where(xlo == 0, other, probes)])
    other = lax.ppermute(by_xlo, "core", pair)
    chip = jnp.stack([jnp.where(core == 0, by_xlo, other), jnp.where(core == 0, other, by_xlo)], axis=1)
    chip = chip.reshape(2, 2 * probes.shape[0], probes.shape[1])
    half = lax.dynamic_index_in_dim(chip, core, 0, keepdims=False)

    def hops(step, count):
        perm = [(r, ((r // 4 + step) % nz) * 4 + r % 4) for r in range(runs)]
        out, cur = [], half
        for _ in range(count):
            cur = lax.ppermute(cur, RUN, perm)
            out.append(cur)
        return out

    ahead, behind = hops(1, nz // 2), hops(-1, (nz - 1) // 2)
    mine = [half] + ahead + behind
    where_from = [z] + [(z - k) % nz for k in range(1, len(ahead) + 1)] + [(z + k) % nz for k in range(1, len(behind) + 1)]
    theirs = lax.ppermute(jnp.stack(mine), "core", pair)
    full = jnp.zeros((nz,) + chip.shape, chip.dtype)
    zero = jnp.zeros((), z.dtype)
    for j, zi in enumerate(where_from):
        full = lax.dynamic_update_slice(full, mine[j][None, None], (zi, core, zero, zero))
        full = lax.dynamic_update_slice(full, theirs[j][None, None], (zi, 1 - core, zero, zero))
    return jnp.dot(gradients, full.reshape(-1, probes.shape[1]), preferred_element_type=jnp.float32)


def per_device(runs, entries, gradients, probes):
    run_bits = list(range(runs.bit_length() - 1))
    partial_sketch = gathered_sketch(gradients, probes, runs)
    sketch = all_reduce_halving(partial_sketch, ENTRY, entries, [(entries // 2).bit_length() - 1], "y", entries // 2)
    local_gram = jnp.dot(
        sketch.T, sketch, precision=HI, preferred_element_type=jnp.float32
    )
    gram = all_reduce_halving(local_gram, RUN, runs, [0, 1], "z", runs // 4)
    inv = inverse_factor(gram)
    basis = jnp.dot(sketch, inv.T, precision=HI).astype(jnp.bfloat16)
    return reduce_scatter_projection(basis, gradients, runs)


def reduce_scatter_projection(basis, gradients, runs):
    nz = runs // 4
    probes = basis.shape[1]
    rows = probes // runs
    idx = lax.axis_index(RUN)
    core = idx % 2
    xlo = (idx // 2) % 2
    z = idx // 4
    cols = basis.reshape(basis.shape[0], nz, 2, 2, rows)

    def project(c):
        b = lax.dynamic_index_in_dim(cols, c, 3, keepdims=False).reshape(basis.shape[0], -1)
        out = lax.dot_general(b, gradients, (((0,), (0,)), ((), ())), preferred_element_type=jnp.float32)
        return out.reshape(nz, 2, rows, gradients.shape[1])

    sent = project(1 - core)
    got = lax.ppermute(sent, RUN, [(i, i ^ 1) for i in range(runs)])
    own = project(core)

    split = rows // 2

    def ring(x, r0, step_sign):
        perm = [(i, (i + 4 * step_sign) % runs) for i in range(runs)]

        def part(d):
            return own[d, x, r0:r0 + split] + got[d, x, r0:r0 + split]

        acc = None
        for s in range(nz - 1):
            d = (z - step_sign * (1 + s)) % nz
            acc = lax.ppermute(part(d) if acc is None else acc + part(d), RUN, perm)
        return acc + part(z)

    lo = jnp.concatenate([ring(0, 0, 1), ring(0, split, 1)], axis=0)
    hi = jnp.concatenate([ring(1, 0, -1), ring(1, split, -1)], axis=0)
    keep = jnp.where(xlo == 0, lo, hi)
    send = jnp.where(xlo == 0, hi, lo)
    return keep + lax.ppermute(send, RUN, [(i, i ^ 2) for i in range(runs)])


def solution(mesh):
    runs, entries = mesh.shape["run"], mesh.shape["entry"]
    split = jax.sharding.Mesh(mesh.devices.reshape(runs // 4, 2, 2, 2, entries // 2), RUN + ENTRY)
    placed = (P(RUN, ENTRY), P(ENTRY + RUN, None))
    body = functools.partial(per_device, runs, entries)
    return jax.shard_map(
        body, mesh=split, in_specs=placed, out_specs=P(RUN, ENTRY), check_vma=False
    )
```
